32 devices in a mesh: groups: 2 (over y), ctx: 4 (over x, core), dp: 4 (over z).
Axes of the slice: x: 2, y: 2, z: 4, core: 2. Of those that a mesh axis runs over, the one named last changes fastest.
Arguments:
- hidden_in: bfloat16 [8192, 1536], P(('groups', 'ctx', 'dp')), parts along dimension 0, may hold values from -0.119628906 to 0.119628906
- queries: bfloat16 [8192, 1536], P(('groups', 'ctx', 'dp')), parts along dimension 0, may hold values from -60 to 60
- keys: bfloat16 [8192, 256], P(('groups', 'ctx', 'dp')), parts along dimension 0, may hold values from -60 to 60
- values: bfloat16 [8192, 256], P(('groups', 'ctx', 'dp')), parts along dimension 0, may hold values from -6 to 6
- out_grad: bfloat16 [8192, 1536], P(('groups', 'ctx', 'dp')), parts along dimension 0, may hold values from -48 to 48
- segment_ids: int32 [8192], P('groups'), parts along dimension 0, may hold values from 0 to 15, never falling along the last dimension, each value on 1 to 512 neighbouring positions
Outputs:
- query_grad: bfloat16 [8192, 1536], P(('groups', 'ctx', 'dp')), parts along dimension 0
- kv_weight_grad: float32 [3072, 512], P(('groups', 'dp')), parts along dimension 0
The draws below stay inside these ranges and needn't reach their ends.
There are 2 independent parts, one for each index of `groups`. The reference program is written for one: setup_inputs(seed, part) draws one part's arguments, and reference() takes and returns one part's arrays. A program takes and returns all parts, laid end to end along the dimension named above; each array names one. Nothing has to cross between parts.
Inputs may be any that keep to these rules, and one draw needn't show every extreme that they name: `segment_ids`: the ids never fall along the tokens; each rollout takes 1 to 512 consecutive positions, and one takes exactly 512.
All inputs are finite; a program needn't handle non-finite values.
Results may differ from the reference program's by a relative error of at most 0.0049.
Values may be sent and summed in bfloat16 or wider, within the bound.
No kernel may reach another device: no remote copies, remote signals or barrier semaphores. Data moves between devices by JAX's collectives and lax.ppermute only.
A program may use at most 64 MiB of HBM per device.

```python
import math
import jax
import jax.numpy as jnp
import numpy as np
from jax import lax

D = 1536
QUERY_HEADS = 12
KEY_VALUE_HEADS = 2
HEAD_SIZE = 128
BLOCK_TOKENS = 256
SEGS = 16
PACK_TOKENS = 4096
MOST = 512


def shared_keys(key):
    target_shape = (PACK_TOKENS, KEY_VALUE_HEADS * HEAD_SIZE)
    result = jax.random.truncated_normal(jax.random.fold_in(key, 21), -6.0, 6.0, target_shape, jnp.float32)
    return result


def draw_keys(key, part):
    return shared_keys(key).astype(jnp.bfloat16)


def draw_queries(key, part):
    group_width = QUERY_HEADS // KEY_VALUE_HEADS
    target_shape = (PACK_TOKENS, KEY_VALUE_HEADS, group_width, HEAD_SIZE)
    result = jax.random.truncated_normal(jax.random.fold_in(key, 31), -6.0, 6.0, target_shape, jnp.float32)
    return result.reshape(PACK_TOKENS, QUERY_HEADS * HEAD_SIZE).astype(jnp.bfloat16)


def with_spikes(drawn, key, source, target, blocks, factor):
    def block_of(dim):
        return (jnp.arange(drawn.shape[dim]) // (drawn.shape[dim] // blocks)).reshape((-1,) + (1,) * (drawn.ndim - 1 - dim))

    near = jax.random.permutation(key, blocks)[block_of(target)]
    other_side = (block_of(target) + blocks // 2) % blocks
    return jnp.where((block_of(source) == near) | (block_of(source) == other_side), factor * drawn, drawn)


def shard_levels(key, dims, pieces, smallest, largest):
    def one(position, shards_of):
        steps = jax.random.uniform(jax.random.fold_in(jax.random.fold_in(key, 6), position), (shards_of,), jnp.float32, smallest / len(pieces), largest / len(pieces))
        return jnp.repeat(jnp.exp(steps), dims[position] // shards_of).reshape((-1,) + (1,) * (len(dims) - position - 1))

    level = one(*pieces[0])
    for cut in pieces[1:]:
        level = level * one(*cut)
    return level


def profile(count, total, bound, skew):
    loads = [(1 << 20) // math.isqrt(grade ** skew) + 1 for grade in range(2, count + 1)]
    surplus, given = total - bound - (count - 1), [1] * (count - 1)
    while surplus > 0:
        movable = [i for i in range(count - 1) if given[i] < bound]
        whole, left = sum([loads[i] for i in movable]), surplus
        for i in movable:
            extra = min(bound - given[i], max(1, left * loads[i] // whole), surplus)
            given[i] = given[i] + extra
            surplus = surplus - extra
    return np.array([bound] + given)


def ragged(rng, amount, total, most, skew):
    if amount == 2:
        one = jax.random.randint(rng, (), max(1, total - most), min(most, total - 1) + 1)
        return jnp.stack([one, total - one])
    lengths = jnp.asarray(profile(amount, total, most, skew), jnp.int32)
    pairs = (amount - 1) // 2
    giver, taker = lengths[1:1 + 2 * pairs:2], lengths[2:2 + 2 * pairs:2]
    slack = jnp.minimum(giver - 1, most - taker)
    moved = jax.random.randint(jax.random.fold_in(rng, 1), (pairs,), 0, 1 << 20) % (slack + 1)
    lengths = lengths.at[1:1 + 2 * pairs:2].set(giver - moved).at[2:2 + 2 * pairs:2].set(taker + moved)
    return lengths[jax.random.permutation(jax.random.fold_in(rng, 2), amount)]


def scatter_about(rng, dims, width, bound, cuts=(), kind=jnp.bfloat16):
    entries = jax.random.normal(rng, dims, jnp.float32) * width
    if len(cuts) > 0:
        entries = shard_levels(rng, dims, cuts, -0.22, 0.18) * entries
    return jnp.clip(entries, min=-bound, max=bound).astype(kind)


def bell_draw_with(key, shape, deviation, reach, shards, heavy, kind=jnp.bfloat16):
    values = deviation * jax.random.normal(key, shape, jnp.float32)
    if shards:
        values = values * shard_levels(key, shape, shards, -0.22, 0.18)
    return jnp.clip(with_spikes(values, jax.random.fold_in(key, 3), *heavy), -reach, reach).astype(kind)


def setup_inputs(seed: int = 0, part: int = 0) -> dict:
    streams_of = jax.random.split(jax.random.key(seed), 7)
    own_keys = jax.random.split(jax.random.fold_in(streams_of[6], part), 7)
    hidden_in = bell_draw_with(own_keys[0], (PACK_TOKENS, D), 0.02, 0.119628906, ((0, 16),), (0, 1, 16, 2.0))
    queries = draw_queries(jax.random.fold_in(jax.random.fold_in(streams_of[6], part), 71), part)
    keys = draw_keys(jax.random.fold_in(jax.random.fold_in(streams_of[6], part), 71), part)
    values = scatter_about(own_keys[3], (PACK_TOKENS, KEY_VALUE_HEADS * HEAD_SIZE), 1.0, 6.0, ((0, 16),))
    out_grad = scatter_about(own_keys[4], (PACK_TOKENS, QUERY_HEADS * HEAD_SIZE), 8.0, 48.0, ((0, 16),))
    segment_ids = jnp.searchsorted(jnp.cumsum(ragged(own_keys[5], SEGS, PACK_TOKENS, MOST, 1)), jnp.arange(PACK_TOKENS), side="right").astype(jnp.int32)
    return dict(hidden_in=hidden_in, queries=queries, keys=keys, values=values, out_grad=out_grad, segment_ids=segment_ids)


def block_grads(block_of_query, key_span_window, value_span_window, block_gradient, visible):
    rows_per_block = block_of_query.shape[0]
    rows_in_span = key_span_window.shape[0]
    group_width = QUERY_HEADS // KEY_VALUE_HEADS
    scale = HEAD_SIZE ** -0.5
    heads_of_query = block_of_query.astype(jnp.float32).reshape(rows_per_block, KEY_VALUE_HEADS, group_width, HEAD_SIZE)
    head_gradients = block_gradient.astype(jnp.float32).reshape(rows_per_block, KEY_VALUE_HEADS, group_width, HEAD_SIZE)
    heads_of_key = key_span_window.astype(jnp.float32).reshape(rows_in_span, KEY_VALUE_HEADS, HEAD_SIZE)
    heads_of_value = value_span_window.astype(jnp.float32).reshape(rows_in_span, KEY_VALUE_HEADS, HEAD_SIZE)
    query_parts = []
    key_pieces = []
    value_pieces = []
    for head_position in range(KEY_VALUE_HEADS):
        query_now = heads_of_query[:, head_position]
        grad_now = head_gradients[:, head_position]
        key_now = heads_of_key[:, head_position]
        value_now = heads_of_value[:, head_position]
        scores = jnp.einsum("tgd,sd->gts", query_now, key_now) * scale
        scores = jnp.where(visible[None], scores, -jnp.inf)
        top = jnp.max(scores, axis=-1, keepdims=True)
        expo = jnp.exp(scores - top)
        probs = expo / jnp.sum(expo, axis=-1, keepdims=True)
        probs_low = lax.optimization_barrier(probs.astype(jnp.bfloat16)).astype(jnp.float32)
        dprobs = jnp.einsum("tgd,sd->gts", grad_now, value_now)
        delta = jnp.sum(probs * dprobs, axis=-1, keepdims=True)
        dscores = probs * (dprobs - delta)
        dscores_low = lax.optimization_barrier(dscores.astype(jnp.bfloat16)).astype(jnp.float32)
        value_pieces.append(jnp.einsum("gts,tgd->sd", probs_low, grad_now))
        key_pieces.append(jnp.einsum("gts,tgd->sd", dscores_low, query_now) * scale)
        query_parts.append(jnp.einsum("gts,sd->tgd", dscores_low, key_now) * scale)
    query_grad = jnp.stack(query_parts, 1).reshape(rows_per_block, QUERY_HEADS * HEAD_SIZE)
    key_gradient = jnp.stack(key_pieces, 1).reshape(rows_in_span, KEY_VALUE_HEADS * HEAD_SIZE)
    value_gradient = jnp.stack(value_pieces, 1).reshape(rows_in_span, KEY_VALUE_HEADS * HEAD_SIZE)
    return query_grad, jnp.concatenate([key_gradient, value_gradient], 1)


def reference(hidden_in, queries, keys, values, out_grad, segment_ids):
    blocks = PACK_TOKENS // BLOCK_TOKENS
    column_span = 2 * KEY_VALUE_HEADS * HEAD_SIZE
    segment_pack = segment_ids.astype(jnp.int32)
    padded_keys = jnp.concatenate([jnp.zeros((BLOCK_TOKENS, KEY_VALUE_HEADS * HEAD_SIZE), keys.dtype), keys], 0)
    padded_values = jnp.concatenate([jnp.zeros((BLOCK_TOKENS, KEY_VALUE_HEADS * HEAD_SIZE), values.dtype), values], 0)
    segment_padded = jnp.concatenate([jnp.zeros((BLOCK_TOKENS,), jnp.int32), segment_pack], 0)
    query_rows = jnp.arange(BLOCK_TOKENS, dtype=jnp.int32)[:, None]
    key_cols = jnp.arange(2 * BLOCK_TOKENS, dtype=jnp.int32)[None, :]

    def one_block(block_index):
        start = (block_index * BLOCK_TOKENS).astype(jnp.int32)
        block_of_query = lax.dynamic_slice_in_dim(queries, start, BLOCK_TOKENS, 0)
        block_gradient = lax.dynamic_slice_in_dim(out_grad, start, BLOCK_TOKENS, 0)
        key_span_window = lax.dynamic_slice_in_dim(padded_keys, start, 2 * BLOCK_TOKENS, 0)
        value_span_window = lax.dynamic_slice_in_dim(padded_values, start, 2 * BLOCK_TOKENS, 0)
        own_segments = lax.dynamic_slice_in_dim(segment_pack, start, BLOCK_TOKENS, 0)
        key_segments = lax.dynamic_slice_in_dim(segment_padded, start, 2 * BLOCK_TOKENS, 0)
        visible = (key_cols <= query_rows + BLOCK_TOKENS) & ((key_cols >= BLOCK_TOKENS) | (block_index > 0))
        visible = visible & (key_segments[None, :] == own_segments[:, None])
        return block_grads(block_of_query, key_span_window, value_span_window, block_gradient, visible)

    query_blocks, window_grads = lax.map(one_block, jnp.arange(blocks, dtype=jnp.int32))
    own_part = window_grads[:, BLOCK_TOKENS:]
    next_part = jnp.concatenate([window_grads[1:, :BLOCK_TOKENS], jnp.zeros((1, BLOCK_TOKENS, column_span), jnp.float32)], 0)
    kv_grad = (own_part + next_part).reshape(PACK_TOKENS, column_span)
    weight_grad = jnp.einsum("td,tc->dc", hidden_in.astype(jnp.float32), kv_grad, precision=lax.Precision.HIGHEST)
    return query_blocks.reshape(PACK_TOKENS, QUERY_HEADS * HEAD_SIZE).astype(jnp.bfloat16), weight_grad
```

```python
import jax
import jax.numpy as jnp
from jax import lax
from jax.sharding import PartitionSpec as P

QUERY_HEADS = 12
KEY_VALUE_HEADS = 2
HEAD_SIZE = 128


def shifted(block, axis, distance):
    devices = range(lax.axis_size(axis))
    route = [(i - distance, i) for i in devices if i - distance in devices]
    return lax.ppermute(block, axis, route)


def exchange(block, axis, bit):
    count = lax.axis_size(axis)
    return lax.ppermute(block, axis, [(i, i ^ bit) for i in range(count)])


def halving_scatter(chunks, axis):
    count = lax.axis_size(axis)
    place = lax.axis_index(axis)
    bit = 1
    while bit < count:
        pairs = chunks.reshape((chunks.shape[0] // 2, 2) + chunks.shape[1:])
        side = (place // bit) % 2
        kept = lax.dynamic_index_in_dim(pairs, side, 1, keepdims=False)
        sent = lax.dynamic_index_in_dim(pairs, 1 - side, 1, keepdims=False)
        chunks = kept + exchange(sent, axis, bit)
        bit *= 2
    return chunks[0]


def doubling_gather(chunk, axis):
    count = lax.axis_size(axis)
    place = lax.axis_index(axis)
    held = chunk[None]
    bit = count // 2
    while bit >= 1:
        other = exchange(held, axis, bit)
        side = (place // bit) % 2
        low = jnp.where(side == 0, held, other)
        high = jnp.where(side == 0, other, held)
        held = jnp.stack([low, high], 1).reshape((held.shape[0] * 2,) + held.shape[1:])
        bit //= 2
    return held


def spread_sum(term):
    ctx_count = lax.axis_size("ctx")
    dp_count = lax.axis_size("dp")
    cols = term.shape[1]
    piece = term.shape[0] // (ctx_count * dp_count)
    by_ctx = term.reshape(dp_count, ctx_count, piece, cols).transpose(1, 0, 2, 3)
    over_ctx = halving_scatter(by_ctx, "ctx")
    over_all = halving_scatter(over_ctx, "dp")
    return doubling_gather(over_all, "ctx").reshape(ctx_count * piece, cols)


def window_grads(block_of_query, key_span_window, value_span_window, block_gradient, visible):
    rows_per_block = block_of_query.shape[0]
    rows_in_span = key_span_window.shape[0]
    group_width = QUERY_HEADS // KEY_VALUE_HEADS
    scale = HEAD_SIZE ** (-0.5)
    heads_of_query = block_of_query.reshape(rows_per_block, KEY_VALUE_HEADS, group_width, HEAD_SIZE)
    head_gradients = block_gradient.reshape(rows_per_block, KEY_VALUE_HEADS, group_width, HEAD_SIZE)
    heads_of_key = key_span_window.reshape(rows_in_span, KEY_VALUE_HEADS, HEAD_SIZE)
    heads_of_value = value_span_window.reshape(rows_in_span, KEY_VALUE_HEADS, HEAD_SIZE)
    query_parts = []
    key_pieces = []
    value_pieces = []
    for head_position in range(KEY_VALUE_HEADS):
        query_now = heads_of_query[:, head_position]
        grad_now = head_gradients[:, head_position]
        key_now = heads_of_key[:, head_position]
        value_now = heads_of_value[:, head_position]
        scores = (
            jnp.einsum("tgd,sd->gts", query_now, key_now, preferred_element_type=jnp.float32)
            * scale
        )
        scores = jnp.where(visible[None], scores, -jnp.inf)
        top = jnp.max(scores, axis=-1, keepdims=True)
        expo = jnp.exp(scores - top)
        probs = expo / jnp.sum(expo, axis=-1, keepdims=True)
        probs_low = probs.astype(jnp.bfloat16)
        dprobs = jnp.einsum("tgd,sd->gts", grad_now, value_now, preferred_element_type=jnp.float32)
        delta = jnp.sum(probs * dprobs, axis=-1, keepdims=True)
        dscores_low = (probs * (dprobs - delta)).astype(jnp.bfloat16)
        value_pieces.append(
            jnp.einsum("gts,tgd->sd", probs_low, grad_now, preferred_element_type=jnp.float32)
        )
        key_pieces.append(
            jnp.einsum("gts,tgd->sd", dscores_low, query_now, preferred_element_type=jnp.float32)
            * scale
        )
        query_parts.append(
            jnp.einsum("gts,sd->tgd", dscores_low, key_now, preferred_element_type=jnp.float32)
            * scale
        )
    query_grad = jnp.stack(query_parts, 1).reshape(rows_per_block, QUERY_HEADS * HEAD_SIZE)
    key_gradient = jnp.stack(key_pieces, 1).reshape(rows_in_span, KEY_VALUE_HEADS * HEAD_SIZE)
    value_gradient = jnp.stack(value_pieces, 1).reshape(rows_in_span, KEY_VALUE_HEADS * HEAD_SIZE)
    return (query_grad, jnp.concatenate([key_gradient, value_gradient], 1))


def weight_term(hidden_block, kv_grad):
    high = kv_grad.astype(jnp.bfloat16)
    low = (kv_grad - high.astype(jnp.float32)).astype(jnp.bfloat16)
    both = jnp.einsum(
        "td,tc->dc", hidden_block, jnp.concatenate([high, low], 1), preferred_element_type=jnp.float32
    )
    cols = kv_grad.shape[1]
    return both[:, :cols] + both[:, cols:]


def on_device(hidden_in, queries, keys, values, out_grad, segment_ids):
    rows_per_block = queries.shape[0]
    cycle_place = lax.axis_index(("ctx", "dp"))
    prev_keys, prev_values = shifted((keys, values), ("ctx", "dp"), 1)
    key_span_window = jnp.concatenate([prev_keys, keys], 0)
    value_span_window = jnp.concatenate([prev_values, values], 0)
    own_segments = lax.dynamic_slice_in_dim(
        segment_ids, cycle_place * rows_per_block, rows_per_block, 0
    )
    prev_segments = lax.dynamic_slice_in_dim(
        segment_ids, jnp.maximum(cycle_place - 1, 0) * rows_per_block, rows_per_block, 0
    )
    key_segments = jnp.concatenate([prev_segments, own_segments], 0)
    query_rows = jnp.arange(rows_per_block, dtype=jnp.int32)[:, None]
    key_cols = jnp.arange(2 * rows_per_block, dtype=jnp.int32)[None, :]
    visible = (key_cols <= query_rows + rows_per_block) & (
        (key_cols >= rows_per_block) | (cycle_place > 0)
    )
    visible = visible & (key_segments[None, :] == own_segments[:, None])
    query_grad, kv_window = window_grads(
        queries, key_span_window, value_span_window, out_grad, visible
    )
    returned = shifted(kv_window[:rows_per_block].astype(jnp.bfloat16), ("ctx", "dp"), -1).astype(
        jnp.float32
    )
    term = weight_term(hidden_in, kv_window[rows_per_block:] + returned)
    total_rows = term.shape[0]
    replica_count = lax.axis_size("dp")
    weight_grad = spread_sum(term)
    return (query_grad.astype(jnp.bfloat16), weight_grad)


def solution(mesh):
    return jax.shard_map(
        on_device,
        mesh=mesh,
        in_specs=(
            P(("groups", "ctx", "dp"), None),
            P(("groups", "ctx", "dp"), None),
            P(("groups", "ctx", "dp"), None),
            P(("groups", "ctx", "dp"), None),
            P(("groups", "ctx", "dp"), None),
            P("groups"),
        ),
        out_specs=(P(("groups", "ctx", "dp"), None), P(("groups", "dp"), None)),
        check_vma=False,
    )
```

```python
import jax
import jax.numpy as jnp
from jax import lax
from jax.sharding import PartitionSpec as P

QUERY_HEADS = 12
KEY_VALUE_HEADS = 2
HEAD_SIZE = 128


def shifted(block, axis, distance):
    devices = range(lax.axis_size(axis))
    route = [(i - distance, i) for i in devices if i - distance in devices]
    return lax.ppermute(block, axis, route)


def exchange(block, axis, bit):
    count = lax.axis_size(axis)
    return lax.ppermute(block, axis, [(i, i ^ bit) for i in range(count)])


def bits_of(count):
    width = count.bit_length() - 1
    assert 1 << width == count
    return width


def halving_scatter(chunks, axis, first_sent=None):
    count = lax.axis_size(axis)
    place = lax.axis_index(axis)
    bit = 1
    while bit < count:
        side = (place // bit) % 2
        if first_sent is None:
            kept = lax.dynamic_index_in_dim(chunks, side, 0, keepdims=False)
            sent = lax.dynamic_index_in_dim(chunks, 1 - side, 0, keepdims=False)
        else:
            kept, sent = chunks, first_sent
            first_sent = None
        chunks = kept + exchange(sent, axis, bit)
        bit *= 2
    return chunks


def doubling_gather(chunk, axis):
    count = lax.axis_size(axis)
    place = lax.axis_index(axis)
    held = chunk[None]
    bit = count // 2
    while bit >= 1:
        other = exchange(held, axis, bit)
        side = (place // bit) % 2
        low = jnp.where(side == 0, held, other)
        high = jnp.where(side == 0, other, held)
        held = jnp.stack([low, high], 1).reshape((held.shape[0] * 2,) + held.shape[1:])
        bit //= 2
    return held


def split_hi_lo(values):
    high = values.astype(jnp.bfloat16)
    rest = values - lax.reduce_precision(values, exponent_bits=8, mantissa_bits=7)
    return jnp.concatenate([high, rest.astype(jnp.bfloat16)], 1)


def weight_rows(hidden_cols, kv_parts):
    both = jnp.einsum("td,tc->dc", hidden_cols, kv_parts, preferred_element_type=jnp.float32)
    cols = kv_parts.shape[1] // 2
    return both[:, :cols] + both[:, cols:]


def routed_scatter(halves, labels, schedules):
    labels = [list(labels) for _ in halves]
    halves = list(halves)
    for step in range(len(schedules[0])):
        sends = {}
        for h, schedule in enumerate(schedules):
            axis, bit = schedule[step]
            at = labels[h].index((axis, bit))
            side = (lax.axis_index(axis) // bit) % 2
            kept = lax.dynamic_index_in_dim(halves[h], side, at, keepdims=False)
            sent = lax.dynamic_index_in_dim(halves[h], 1 - side, at, keepdims=False)
            labels[h].pop(at)
            halves[h] = kept
            sends.setdefault((axis, bit), []).append((h, sent))
        for (axis, bit), items in sends.items():
            if len(items) == 1:
                got = [exchange(items[0][1], axis, bit)]
            else:
                got = exchange(jnp.stack([x for _, x in items]), axis, bit)
                got = [got[k] for k in range(len(items))]
            for (h, _), g in zip(items, got):
                halves[h] = halves[h] + g
    return halves


def weight_grad_of(hidden_window, kv_window):
    ctx_count = lax.axis_size("ctx")
    dp_count = lax.axis_size("dp")
    ctx_bits = bits_of(ctx_count)
    dp_bits = bits_of(dp_count)
    tokens, width = hidden_window.shape
    cols = kv_window.shape[1]
    piece = width // (ctx_count * dp_count)
    split = hidden_window.reshape((tokens,) + (2,) * (dp_bits + ctx_bits) + (piece,))
    d_axes = list(range(1, 1 + dp_bits))
    c_axes = list(range(1 + dp_bits, 1 + dp_bits + ctx_bits))
    order = [0] + c_axes[::-1] + d_axes[::-1] + [1 + dp_bits + ctx_bits]
    hidden_cols = split.transpose(order).reshape(tokens, 2, width // 2)
    kv_parts = split_hi_lo(kv_window)
    side = lax.axis_index("ctx") % 2
    sent_cols = lax.dynamic_index_in_dim(hidden_cols, 1 - side, 1, keepdims=False)
    kept_cols = lax.dynamic_index_in_dim(hidden_cols, side, 1, keepdims=False)
    lead = (2,) * (ctx_bits + dp_bits - 1) + (piece, cols)
    sent = weight_rows(sent_cols, kv_parts).reshape(lead)
    kept = weight_rows(kept_cols, kv_parts).reshape(lead)
    summed = kept + exchange(sent, "ctx", 1)
    ctx_rest = [("ctx", 1 << k) for k in range(1, ctx_bits)]
    dp_all = [("dp", 1 << k) for k in range(dp_bits)]
    labels = ctx_rest + dp_all
    if dp_all and ctx_rest:
        first = ctx_rest + dp_all
        second = dp_all[:1] + ctx_rest + dp_all[1:]
        half = cols // 2
        parts = routed_scatter(
            [summed[..., :half], summed[..., half:]], labels, [first, second]
        )
        over_all = jnp.concatenate(parts, -1)
    else:
        over_all = routed_scatter([summed], labels, [labels])[0]
    return doubling_gather(over_all, "ctx").reshape(ctx_count * piece, cols)


def window_grads(block_of_query, key_span_window, value_span_window, block_gradient, visible):
    rows_per_block = block_of_query.shape[0]
    rows_in_span = key_span_window.shape[0]
    group_width = QUERY_HEADS // KEY_VALUE_HEADS
    scale = HEAD_SIZE ** (-0.5)
    heads_of_query = block_of_query.reshape(rows_per_block, KEY_VALUE_HEADS, group_width, HEAD_SIZE)
    head_gradients = block_gradient.reshape(rows_per_block, KEY_VALUE_HEADS, group_width, HEAD_SIZE)
    heads_of_key = key_span_window.reshape(rows_in_span, KEY_VALUE_HEADS, HEAD_SIZE)
    heads_of_value = value_span_window.reshape(rows_in_span, KEY_VALUE_HEADS, HEAD_SIZE)
    query_parts = []
    key_pieces = []
    value_pieces = []
    for head_position in range(KEY_VALUE_HEADS):
        query_now = heads_of_query[:, head_position]
        grad_now = head_gradients[:, head_position]
        key_now = heads_of_key[:, head_position]
        value_now = heads_of_value[:, head_position]
        scores = (
            jnp.einsum("tgd,sd->gts", query_now, key_now, preferred_element_type=jnp.float32)
            * scale
        )
        scores = jnp.where(visible[None], scores, -jnp.inf)
        top = jnp.max(scores, axis=-1, keepdims=True)
        expo = jnp.exp(scores - top)
        probs = expo / jnp.sum(expo, axis=-1, keepdims=True)
        probs_low = probs.astype(jnp.bfloat16)
        dprobs = jnp.einsum("tgd,sd->gts", grad_now, value_now, preferred_element_type=jnp.float32)
        delta = jnp.sum(probs * dprobs, axis=-1, keepdims=True)
        dscores_low = (probs * (dprobs - delta)).astype(jnp.bfloat16)
        value_pieces.append(
            jnp.einsum("gts,tgd->sd", probs_low, grad_now, preferred_element_type=jnp.float32)
        )
        key_pieces.append(
            jnp.einsum("gts,tgd->sd", dscores_low, query_now, preferred_element_type=jnp.float32)
            * scale
        )
        query_parts.append(
            jnp.einsum("gts,sd->tgd", dscores_low, key_now, preferred_element_type=jnp.float32)
            * scale
        )
    query_grad = jnp.stack(query_parts, 1).reshape(rows_per_block, QUERY_HEADS * HEAD_SIZE)
    key_gradient = jnp.stack(key_pieces, 1).reshape(rows_in_span, KEY_VALUE_HEADS * HEAD_SIZE)
    value_gradient = jnp.stack(value_pieces, 1).reshape(rows_in_span, KEY_VALUE_HEADS * HEAD_SIZE)
    return (query_grad, jnp.concatenate([key_gradient, value_gradient], 1))


def on_device(hidden_in, queries, keys, values, out_grad, segment_ids):
    rows_per_block = queries.shape[0]
    cycle_place = lax.axis_index(("ctx", "dp"))
    kv_width = keys.shape[1]
    prev_kv = shifted(jnp.concatenate([keys, values], 1), ("ctx", "dp"), 1)
    prev_hidden = shifted(hidden_in, ("ctx", "dp"), 1)
    key_span_window = jnp.concatenate([prev_kv[:, :kv_width], keys], 0)
    value_span_window = jnp.concatenate([prev_kv[:, kv_width:], values], 0)
    own_segments = lax.dynamic_slice_in_dim(
        segment_ids, cycle_place * rows_per_block, rows_per_block, 0
    )
    prev_segments = lax.dynamic_slice_in_dim(
        segment_ids, jnp.maximum(cycle_place - 1, 0) * rows_per_block, rows_per_block, 0
    )
    key_segments = jnp.concatenate([prev_segments, own_segments], 0)
    query_rows = jnp.arange(rows_per_block, dtype=jnp.int32)[:, None]
    key_cols = jnp.arange(2 * rows_per_block, dtype=jnp.int32)[None, :]
    visible = (key_cols <= query_rows + rows_per_block) & (
        (key_cols >= rows_per_block) | (cycle_place > 0)
    )
    visible = visible & (key_segments[None, :] == own_segments[:, None])
    query_grad, kv_window = window_grads(
        queries, key_span_window, value_span_window, out_grad, visible
    )
    hidden_window = jnp.concatenate([prev_hidden, hidden_in], 0)
    weight_grad = weight_grad_of(hidden_window, kv_window)
    return (query_grad.astype(jnp.bfloat16), weight_grad)


def solution(mesh):
    return jax.shard_map(
        on_device,
        mesh=mesh,
        in_specs=(
            P(("groups", "ctx", "dp"), None),
            P(("groups", "ctx", "dp"), None),
            P(("groups", "ctx", "dp"), None),
            P(("groups", "ctx", "dp"), None),
            P(("groups", "ctx", "dp"), None),
            P("groups"),
        ),
        out_specs=(P(("groups", "ctx", "dp"), None), P(("groups", "dp"), None)),
        check_vma=False,
    )
```

```python
import jax
import jax.numpy as jnp
from jax import lax
from jax.experimental import pallas as pl
from jax.experimental.pallas import tpu as pltpu
from jax.sharding import PartitionSpec as P

QUERY_HEADS = 12
KEY_VALUE_HEADS = 2
HEAD_SIZE = 128


def shifted(block, axis, distance):
    devices = range(lax.axis_size(axis))
    route = [(i - distance, i) for i in devices if i - distance in devices]
    return lax.ppermute(block, axis, route)


def exchange(block, axis, bit):
    count = lax.axis_size(axis)
    return lax.ppermute(block, axis, [(i, i ^ bit) for i in range(count)])


def bits_of(count):
    width = count.bit_length() - 1
    assert 1 << width == count
    return width


def halving_scatter(chunks, axis, first_sent=None):
    count = lax.axis_size(axis)
    place = lax.axis_index(axis)
    bit = 1
    while bit < count:
        side = (place // bit) % 2
        if first_sent is None:
            kept = lax.dynamic_index_in_dim(chunks, side, 0, keepdims=False)
            sent = lax.dynamic_index_in_dim(chunks, 1 - side, 0, keepdims=False)
        else:
            kept, sent = chunks, first_sent
            first_sent = None
        chunks = kept + exchange(sent, axis, bit)
        bit *= 2
    return chunks


def doubling_gather(chunk, axis):
    count = lax.axis_size(axis)
    place = lax.axis_index(axis)
    held = chunk[None]
    bit = count // 2
    while bit >= 1:
        other = exchange(held, axis, bit)
        side = (place // bit) % 2
        low = jnp.where(side == 0, held, other)
        high = jnp.where(side == 0, other, held)
        held = jnp.stack([low, high], 1).reshape((held.shape[0] * 2,) + held.shape[1:])
        bit //= 2
    return held


def split_hi_lo(values):
    high = values.astype(jnp.bfloat16)
    rest = values - lax.reduce_precision(values, exponent_bits=8, mantissa_bits=7)
    return jnp.concatenate([high, rest.astype(jnp.bfloat16)], 1)


def weight_rows(hidden_cols, kv_parts):
    both = jnp.einsum("td,tc->dc", hidden_cols, kv_parts, preferred_element_type=jnp.float32)
    cols = kv_parts.shape[1] // 2
    return both[:, :cols] + both[:, cols:]


def routed_scatter(halves, labels, schedules):
    labels = [list(labels) for _ in halves]
    halves = list(halves)
    for step in range(len(schedules[0])):
        sends = {}
        for h, schedule in enumerate(schedules):
            axis, bit = schedule[step]
            at = labels[h].index((axis, bit))
            side = (lax.axis_index(axis) // bit) % 2
            kept = lax.dynamic_index_in_dim(halves[h], side, at, keepdims=False)
            sent = lax.dynamic_index_in_dim(halves[h], 1 - side, at, keepdims=False)
            labels[h].pop(at)
            halves[h] = kept
            sends.setdefault((axis, bit), []).append((h, sent))
        for (axis, bit), items in sends.items():
            if len(items) == 1:
                got = [exchange(items[0][1], axis, bit)]
            else:
                got = exchange(jnp.stack([x for _, x in items]), axis, bit)
                got = [got[k] for k in range(len(items))]
            for (h, _), g in zip(items, got):
                halves[h] = halves[h] + g
    return halves


def weight_grad_of(hidden_window, kv_window):
    ctx_count = lax.axis_size("ctx")
    dp_count = lax.axis_size("dp")
    ctx_bits = bits_of(ctx_count)
    dp_bits = bits_of(dp_count)
    tokens, width = hidden_window.shape
    cols = kv_window.shape[1]
    piece = width // (ctx_count * dp_count)
    split = hidden_window.reshape((tokens,) + (2,) * (dp_bits + ctx_bits) + (piece,))
    d_axes = list(range(1, 1 + dp_bits))
    c_axes = list(range(1 + dp_bits, 1 + dp_bits + ctx_bits))
    order = [0] + c_axes[::-1] + d_axes[::-1] + [1 + dp_bits + ctx_bits]
    hidden_cols = split.transpose(order).reshape(tokens, 2, width // 2)
    kv_parts = split_hi_lo(kv_window)
    side = lax.axis_index("ctx") % 2
    sent_cols = lax.dynamic_index_in_dim(hidden_cols, 1 - side, 1, keepdims=False)
    kept_cols = lax.dynamic_index_in_dim(hidden_cols, side, 1, keepdims=False)
    lead = (2,) * (ctx_bits + dp_bits - 1) + (piece, cols)
    sent = weight_rows(sent_cols, kv_parts).reshape(lead)
    kept = weight_rows(kept_cols, kv_parts).reshape(lead)
    summed = kept + exchange(sent, "ctx", 1)
    ctx_rest = [("ctx", 1 << k) for k in range(1, ctx_bits)]
    dp_all = [("dp", 1 << k) for k in range(dp_bits)]
    labels = ctx_rest + dp_all
    if dp_all and ctx_rest:
        first = ctx_rest + dp_all
        second = dp_all[:1] + ctx_rest + dp_all[1:]
        half = cols // 2
        parts = routed_scatter(
            [summed[..., :half], summed[..., half:]], labels, [first, second]
        )
        over_all = jnp.concatenate(parts, -1)
    else:
        over_all = routed_scatter([summed], labels, [labels])[0]
    return doubling_gather(over_all, "ctx").reshape(ctx_count * piece, cols)


def attention_kernel(q_ref, g_ref, k_ref, v_ref, qs_ref, ks_ref, dq_ref, dkv_ref):
    rows = q_ref.shape[0]
    span = k_ref.shape[0]
    group_width = QUERY_HEADS // KEY_VALUE_HEADS
    scale = HEAD_SIZE ** (-0.5)
    row = lax.broadcasted_iota(jnp.int32, (rows, span), 0)
    col = lax.broadcasted_iota(jnp.int32, (rows, span), 1)
    visible = (col <= row + rows) & (ks_ref[...] == qs_ref[...])
    kv_cols = KEY_VALUE_HEADS * HEAD_SIZE
    for kv_head in range(KEY_VALUE_HEADS):
        kv_at = pl.ds(kv_head * HEAD_SIZE, HEAD_SIZE)
        key_now = k_ref[:, kv_at]
        value_now = v_ref[:, kv_at]
        key_grad = jnp.zeros((span, HEAD_SIZE), jnp.float32)
        value_grad = jnp.zeros((span, HEAD_SIZE), jnp.float32)
        for member in range(group_width):
            q_at = pl.ds((kv_head * group_width + member) * HEAD_SIZE, HEAD_SIZE)
            query_now = q_ref[:, q_at]
            grad_now = g_ref[:, q_at]
            scores = jnp.einsum("td,sd->ts", query_now, key_now, preferred_element_type=jnp.float32) * scale
            scores = jnp.where(visible, scores, -jnp.inf)
            top = jnp.max(scores, axis=-1, keepdims=True)
            expo = jnp.exp(scores - top)
            probs = expo / jnp.sum(expo, axis=-1, keepdims=True)
            dprobs = jnp.einsum("td,sd->ts", grad_now, value_now, preferred_element_type=jnp.float32)
            delta = jnp.sum(probs * dprobs, axis=-1, keepdims=True)
            dscores_low = (probs * (dprobs - delta)).astype(jnp.bfloat16)
            probs_low = probs.astype(jnp.bfloat16)
            value_grad = value_grad + jnp.einsum("ts,td->sd", probs_low, grad_now, preferred_element_type=jnp.float32)
            key_grad = key_grad + jnp.einsum("ts,td->sd", dscores_low, query_now, preferred_element_type=jnp.float32)
            query_grad = jnp.einsum("ts,sd->td", dscores_low, key_now, preferred_element_type=jnp.float32) * scale
            dq_ref[:, q_at] = query_grad.astype(dq_ref.dtype)
        dkv_ref[:, kv_at] = key_grad * scale
        dkv_ref[:, pl.ds(kv_cols + kv_head * HEAD_SIZE, HEAD_SIZE)] = value_grad


def window_grads(queries, key_window, value_window, out_grad, query_segments, key_segments):
    rows = queries.shape[0]
    span = key_window.shape[0]
    return pl.pallas_call(
        attention_kernel,
        out_shape=(
            jax.ShapeDtypeStruct(queries.shape, jnp.bfloat16),
            jax.ShapeDtypeStruct((span, 2 * key_window.shape[1]), jnp.float32),
        ),
        in_specs=[pl.BlockSpec(memory_space=pltpu.VMEM)] * 6,
        out_specs=(pl.BlockSpec(memory_space=pltpu.VMEM), pl.BlockSpec(memory_space=pltpu.VMEM)),
        cost_estimate=pl.CostEstimate(
            flops=10 * rows * span * QUERY_HEADS * HEAD_SIZE,
            transcendentals=rows * span * QUERY_HEADS,
            bytes_accessed=4 * rows * QUERY_HEADS * HEAD_SIZE * 2 + span * 8 * KEY_VALUE_HEADS * HEAD_SIZE,
        ),
    )(queries, out_grad, key_window, value_window, query_segments.reshape(rows, 1), key_segments.reshape(1, span))


def on_device(hidden_in, queries, keys, values, out_grad, segment_ids):
    rows_per_block = queries.shape[0]
    cycle_place = lax.axis_index(("ctx", "dp"))
    kv_width = keys.shape[1]
    prev_kv = shifted(jnp.concatenate([keys, values], 1), ("ctx", "dp"), 1)
    prev_hidden = shifted(hidden_in, ("ctx", "dp"), 1)
    key_span_window = jnp.concatenate([prev_kv[:, :kv_width], keys], 0)
    value_span_window = jnp.concatenate([prev_kv[:, kv_width:], values], 0)
    own_segments = lax.dynamic_slice_in_dim(
        segment_ids, cycle_place * rows_per_block, rows_per_block, 0
    )
    prev_segments = lax.dynamic_slice_in_dim(
        segment_ids, jnp.maximum(cycle_place - 1, 0) * rows_per_block, rows_per_block, 0
    )
    prev_segments = jnp.where(cycle_place > 0, prev_segments, -1)
    key_segments = jnp.concatenate([prev_segments, own_segments], 0)
    query_grad, kv_window = window_grads(
        queries, key_span_window, value_span_window, out_grad, own_segments, key_segments
    )
    hidden_window = jnp.concatenate([prev_hidden, hidden_in], 0)
    weight_grad = weight_grad_of(hidden_window, kv_window)
    return (query_grad, weight_grad)


def solution(mesh):
    return jax.shard_map(
        on_device,
        mesh=mesh,
        in_specs=(
            P(("groups", "ctx", "dp"), None),
            P(("groups", "ctx", "dp"), None),
            P(("groups", "ctx", "dp"), None),
            P(("groups", "ctx", "dp"), None),
            P(("groups", "ctx", "dp"), None),
            P("groups"),
        ),
        out_specs=(P(("groups", "ctx", "dp"), None), P(("groups", "dp"), None)),
        check_vma=False,
    )
```

```python
import functools

import jax
import jax.numpy as jnp
from jax import lax
from jax.experimental import pallas as pl
from jax.experimental.pallas import tpu as pltpu
from jax.sharding import PartitionSpec as P

QUERY_HEADS = 12
KEY_VALUE_HEADS = 2
HEAD_SIZE = 128


def shifted(block, axis, distance):
    devices = range(lax.axis_size(axis))
    route = [(i - distance, i) for i in devices if i - distance in devices]
    return lax.ppermute(block, axis, route)


def exchange(block, axis, bit):
    count = lax.axis_size(axis)
    return lax.ppermute(block, axis, [(i, i ^ bit) for i in range(count)])


def bits_of(count):
    width = count.bit_length() - 1
    assert 1 << width == count
    return width


def halving_scatter(chunks, axis, first_sent=None):
    count = lax.axis_size(axis)
    place = lax.axis_index(axis)
    bit = 1
    while bit < count:
        side = (place // bit) % 2
        if first_sent is None:
            kept = lax.dynamic_index_in_dim(chunks, side, 0, keepdims=False)
            sent = lax.dynamic_index_in_dim(chunks, 1 - side, 0, keepdims=False)
        else:
            kept, sent = chunks, first_sent
            first_sent = None
        chunks = kept + exchange(sent, axis, bit)
        bit *= 2
    return chunks


def doubling_gather(chunk, axis):
    count = lax.axis_size(axis)
    place = lax.axis_index(axis)
    held = chunk[None]
    bit = count // 2
    while bit >= 1:
        other = exchange(held, axis, bit)
        side = (place // bit) % 2
        low = jnp.where(side == 0, held, other)
        high = jnp.where(side == 0, other, held)
        held = jnp.stack([low, high], 1).reshape((held.shape[0] * 2,) + held.shape[1:])
        bit //= 2
    return held


def split_hi_lo(values):
    high = values.astype(jnp.bfloat16)
    rest = values - lax.reduce_precision(values, exponent_bits=8, mantissa_bits=7)
    return jnp.concatenate([high, rest.astype(jnp.bfloat16)], 1)


def weight_rows(hidden_cols, kv_parts):
    both = jnp.einsum("td,tc->dc", hidden_cols, kv_parts, preferred_element_type=jnp.float32)
    cols = kv_parts.shape[1] // 2
    return both[:, :cols] + both[:, cols:]


def chain_scatter(chunks, labels, schedule):
    labels = list(labels)
    for axis, bit in schedule:
        at = labels.index((axis, bit))
        side = (lax.axis_index(axis) // bit) % 2
        kept = lax.dynamic_index_in_dim(chunks, side, at, keepdims=False)
        sent = lax.dynamic_index_in_dim(chunks, 1 - side, at, keepdims=False)
        labels.pop(at)
        chunks = kept + exchange(sent, axis, bit)
    return chunks


def head_weight_grad(hidden_cols, kv_window, schedule, labels, lead):
    kv_parts = split_hi_lo(kv_window)
    side = lax.axis_index("ctx") % 2
    sent_cols = lax.dynamic_index_in_dim(hidden_cols, 1 - side, 1, keepdims=False)
    kept_cols = lax.dynamic_index_in_dim(hidden_cols, side, 1, keepdims=False)
    sent = weight_rows(sent_cols, kv_parts).reshape(lead + (kv_window.shape[1],))
    kept = weight_rows(kept_cols, kv_parts).reshape(lead + (kv_window.shape[1],))
    summed = kept + exchange(sent, "ctx", 1)
    return doubling_gather(chain_scatter(summed, labels, schedule), "ctx")


def ordered_hidden(hidden_window):
    ctx_bits = bits_of(lax.axis_size("ctx"))
    dp_bits = bits_of(lax.axis_size("dp"))
    tokens, width = hidden_window.shape
    piece = width // (1 << (ctx_bits + dp_bits))
    split = hidden_window.reshape((tokens,) + (2,) * (dp_bits + ctx_bits) + (piece,))
    d_axes = list(range(1, 1 + dp_bits))
    c_axes = list(range(1 + dp_bits, 1 + dp_bits + ctx_bits))
    order = [0] + c_axes[::-1] + d_axes[::-1] + [1 + dp_bits + ctx_bits]
    lead = (2,) * (ctx_bits + dp_bits - 1) + (piece,)
    return split.transpose(order).reshape(tokens, 2, width // 2), lead


def schedules():
    ctx_bits = bits_of(lax.axis_size("ctx"))
    dp_bits = bits_of(lax.axis_size("dp"))
    ctx_rest = [("ctx", 1 << k) for k in range(1, ctx_bits)]
    dp_all = [("dp", 1 << k) for k in range(dp_bits)]
    labels = ctx_rest + dp_all
    second = dp_all[:1] + ctx_rest + dp_all[1:]
    return labels, labels, second


def attention_kernel(kv_heads, q_ref, g_ref, k_ref, v_ref, qs_ref, ks_ref, dq_ref, dkv_ref):
    rows = q_ref.shape[0]
    span = k_ref.shape[0]
    group_width = QUERY_HEADS // KEY_VALUE_HEADS
    scale = HEAD_SIZE ** (-0.5)
    key_row = lax.broadcasted_iota(jnp.int32, (span, rows), 0)
    query_col = lax.broadcasted_iota(jnp.int32, (span, rows), 1)
    visible = (key_row <= query_col + rows) & (ks_ref[...] == qs_ref[...])
    kv_cols = len(kv_heads) * HEAD_SIZE
    for slot, kv_head in enumerate(kv_heads):
        kv_at = pl.ds(kv_head * HEAD_SIZE, HEAD_SIZE)
        key_now = k_ref[:, kv_at]
        value_now = v_ref[:, kv_at]
        key_grad = jnp.zeros((span, HEAD_SIZE), jnp.float32)
        value_grad = jnp.zeros((span, HEAD_SIZE), jnp.float32)
        for member in range(group_width):
            q_at = pl.ds((slot * group_width + member) * HEAD_SIZE, HEAD_SIZE)
            query_now = q_ref[:, q_at]
            grad_now = g_ref[:, q_at]
            scores = jnp.einsum("sd,td->st", key_now, query_now, preferred_element_type=jnp.float32) * scale
            scores = jnp.where(visible, scores, -jnp.inf)
            top = jnp.max(scores, axis=0, keepdims=True)
            expo = jnp.exp(scores - top)
            probs = expo / jnp.sum(expo, axis=0, keepdims=True)
            dprobs = jnp.einsum("sd,td->st", value_now, grad_now, preferred_element_type=jnp.float32)
            delta = jnp.sum(probs * dprobs, axis=0, keepdims=True)
            dscores_low = (probs * (dprobs - delta)).astype(jnp.bfloat16)
            probs_low = probs.astype(jnp.bfloat16)
            value_grad = value_grad + jnp.einsum("st,td->sd", probs_low, grad_now, preferred_element_type=jnp.float32)
            key_grad = key_grad + jnp.einsum("st,td->sd", dscores_low, query_now, preferred_element_type=jnp.float32)
            query_grad = jnp.einsum("st,sd->td", dscores_low, key_now, preferred_element_type=jnp.float32) * scale
            dq_ref[:, q_at] = query_grad.astype(dq_ref.dtype)
        dkv_ref[:, pl.ds(slot * HEAD_SIZE, HEAD_SIZE)] = key_grad * scale
        dkv_ref[:, pl.ds(kv_cols + slot * HEAD_SIZE, HEAD_SIZE)] = value_grad


def window_grads(kv_heads, queries, key_window, value_window, out_grad, query_segments, key_segments):
    rows = queries.shape[0]
    span = key_window.shape[0]
    group_width = QUERY_HEADS // KEY_VALUE_HEADS
    q_cols = len(kv_heads) * group_width * HEAD_SIZE
    kv_cols = len(kv_heads) * HEAD_SIZE
    return pl.pallas_call(
        functools.partial(attention_kernel, kv_heads),
        grid=(1,),
        out_shape=(
            jax.ShapeDtypeStruct((rows, q_cols), jnp.bfloat16),
            jax.ShapeDtypeStruct((span, 2 * kv_cols), jnp.float32),
        ),
        in_specs=[
            pl.BlockSpec((rows, q_cols), lambda i: (0, kv_heads[0] // len(kv_heads))),
            pl.BlockSpec((rows, q_cols), lambda i: (0, kv_heads[0] // len(kv_heads))),
        ] + [pl.BlockSpec(memory_space=pltpu.VMEM)] * 4,
        out_specs=(pl.BlockSpec(memory_space=pltpu.VMEM), pl.BlockSpec(memory_space=pltpu.VMEM)),
        cost_estimate=pl.CostEstimate(
            flops=10 * rows * span * q_cols,
            transcendentals=rows * span * len(kv_heads) * group_width,
            bytes_accessed=4 * rows * q_cols * 2 + span * 8 * kv_cols,
        ),
    )(queries, out_grad, key_window, value_window, query_segments.reshape(1, rows), key_segments.reshape(span, 1))


def on_device(hidden_in, queries, keys, values, out_grad, segment_ids):
    rows_per_block = queries.shape[0]
    cycle_place = lax.axis_index(("ctx", "dp"))
    kv_width = keys.shape[1]
    prev_kv = shifted(jnp.concatenate([keys, values], 1), ("ctx", "dp"), 1)
    prev_hidden = shifted(hidden_in, ("ctx", "dp"), 1)
    key_span_window = jnp.concatenate([prev_kv[:, :kv_width], keys], 0)
    value_span_window = jnp.concatenate([prev_kv[:, kv_width:], values], 0)
    own_segments = lax.dynamic_slice_in_dim(
        segment_ids, cycle_place * rows_per_block, rows_per_block, 0
    )
    prev_segments = lax.dynamic_slice_in_dim(
        segment_ids, jnp.maximum(cycle_place - 1, 0) * rows_per_block, rows_per_block, 0
    )
    prev_segments = jnp.where(cycle_place > 0, prev_segments, -1)
    key_segments = jnp.concatenate([prev_segments, own_segments], 0)
    hidden_cols, lead = ordered_hidden(jnp.concatenate([prev_hidden, hidden_in], 0))
    labels, first, second = schedules()
    query_parts, weight_parts = [], []
    for kv_head in range(KEY_VALUE_HEADS):
        query_part, kv_part = window_grads(
            (kv_head,), queries, key_span_window, value_span_window, out_grad, own_segments, key_segments
        )
        query_parts.append(query_part)
        schedule = first if kv_head % 2 == 0 else second
        weight_parts.append(head_weight_grad(hidden_cols, kv_part, schedule, labels, lead))
    rows = weight_parts[0].shape[0] * weight_parts[0].shape[1]
    weight_parts = [w.reshape(rows, 2, HEAD_SIZE) for w in weight_parts]
    weight_grad = jnp.stack(weight_parts, 2).reshape(rows, 2 * KEY_VALUE_HEADS * HEAD_SIZE)
    return (jnp.concatenate(query_parts, 1), weight_grad)


def solution(mesh):
    return jax.shard_map(
        on_device,
        mesh=mesh,
        in_specs=(
            P(("groups", "ctx", "dp"), None),
            P(("groups", "ctx", "dp"), None),
            P(("groups", "ctx", "dp"), None),
            P(("groups", "ctx", "dp"), None),
            P(("groups", "ctx", "dp"), None),
            P("groups"),
        ),
        out_specs=(P(("groups", "ctx", "dp"), None), P(("groups", "dp"), None)),
        check_vma=False,
    )
```

```python
import functools

import jax
import jax.numpy as jnp
from jax import lax
from jax.experimental import pallas as pl
from jax.experimental.pallas import tpu as pltpu
from jax.sharding import PartitionSpec as P

QUERY_HEADS = 12
KEY_VALUE_HEADS = 2
HEAD_SIZE = 128


def shifted(block, axis, distance):
    devices = range(lax.axis_size(axis))
    route = [(i - distance, i) for i in devices if i - distance in devices]
    return lax.ppermute(block, axis, route)


def exchange(block, axis, bit):
    count = lax.axis_size(axis)
    return lax.ppermute(block, axis, [(i, i ^ bit) for i in range(count)])


def bits_of(count):
    width = count.bit_length() - 1
    assert 1 << width == count
    return width


def halving_scatter(chunks, axis, first_sent=None):
    count = lax.axis_size(axis)
    place = lax.axis_index(axis)
    bit = 1
    while bit < count:
        side = (place // bit) % 2
        if first_sent is None:
            kept = lax.dynamic_index_in_dim(chunks, side, 0, keepdims=False)
            sent = lax.dynamic_index_in_dim(chunks, 1 - side, 0, keepdims=False)
        else:
            kept, sent = chunks, first_sent
            first_sent = None
        chunks = kept + exchange(sent, axis, bit)
        bit *= 2
    return chunks


def doubling_gather(chunk, axis):
    count = lax.axis_size(axis)
    place = lax.axis_index(axis)
    held = chunk[None]
    bit = count // 2
    while bit >= 1:
        other = exchange(held, axis, bit)
        side = (place // bit) % 2
        low = jnp.where(side == 0, held, other)
        high = jnp.where(side == 0, other, held)
        held = jnp.stack([low, high], 1).reshape((held.shape[0] * 2,) + held.shape[1:])
        bit //= 2
    return held


def split_hi_lo(values):
    high = values.astype(jnp.bfloat16)
    rest = values - lax.reduce_precision(values, exponent_bits=8, mantissa_bits=7)
    return jnp.concatenate([high, rest.astype(jnp.bfloat16)], 1)


def weight_rows(hidden_cols, kv_parts):
    both = jnp.einsum("td,tc->dc", hidden_cols, kv_parts, preferred_element_type=jnp.float32)
    cols = kv_parts.shape[1] // 2
    return both[:, :cols] + both[:, cols:]


def chain_scatter(chunks, labels, schedule):
    labels = list(labels)
    for axis, bit in schedule:
        at = labels.index((axis, bit))
        side = (lax.axis_index(axis) // bit) % 2
        kept = lax.dynamic_index_in_dim(chunks, side, at, keepdims=False)
        sent = lax.dynamic_index_in_dim(chunks, 1 - side, at, keepdims=False)
        labels.pop(at)
        chunks = kept + exchange(sent, axis, bit)
    return chunks


def head_weight_grad(hidden_cols, kv_window, schedule, labels, lead):
    kv_parts = split_hi_lo(kv_window)
    side = lax.axis_index("ctx") % 2
    sent_cols = lax.dynamic_index_in_dim(hidden_cols, 1 - side, 1, keepdims=False)
    kept_cols = lax.dynamic_index_in_dim(hidden_cols, side, 1, keepdims=False)
    sent = weight_rows(sent_cols, kv_parts).reshape(lead + (kv_window.shape[1],))
    kept = weight_rows(kept_cols, kv_parts).reshape(lead + (kv_window.shape[1],))
    summed = kept + exchange(sent, "ctx", 1)
    return doubling_gather(chain_scatter(summed, labels, schedule), "ctx")


def ordered_hidden(hidden_window):
    ctx_bits = bits_of(lax.axis_size("ctx"))
    dp_bits = bits_of(lax.axis_size("dp"))
    tokens, width = hidden_window.shape
    piece = width // (1 << (ctx_bits + dp_bits))
    split = hidden_window.reshape((tokens,) + (2,) * (dp_bits + ctx_bits) + (piece,))
    d_axes = list(range(1, 1 + dp_bits))
    c_axes = list(range(1 + dp_bits, 1 + dp_bits + ctx_bits))
    order = [0] + c_axes[::-1] + d_axes[::-1] + [1 + dp_bits + ctx_bits]
    lead = (2,) * (ctx_bits + dp_bits - 1) + (piece,)
    return split.transpose(order).reshape(tokens, 2, width // 2), lead


def schedules():
    ctx_bits = bits_of(lax.axis_size("ctx"))
    dp_bits = bits_of(lax.axis_size("dp"))
    ctx_rest = [("ctx", 1 << k) for k in range(1, ctx_bits)]
    dp_all = [("dp", 1 << k) for k in range(dp_bits)]
    labels = ctx_rest + dp_all
    second = dp_all[:1] + ctx_rest + dp_all[1:]
    return labels, labels, second


def attention_kernel(kv_heads, q_ref, g_ref, k_ref, v_ref, qs_ref, ks_ref, dq_ref, dkv_ref):
    rows = q_ref.shape[0]
    span = k_ref.shape[0]
    group_width = QUERY_HEADS // KEY_VALUE_HEADS
    scale = HEAD_SIZE ** (-0.5)
    key_row = lax.broadcasted_iota(jnp.int32, (span, rows), 0)
    query_col = lax.broadcasted_iota(jnp.int32, (span, rows), 1)
    visible = (key_row <= query_col + rows) & (ks_ref[...] == qs_ref[...])
    kv_cols = len(kv_heads) * HEAD_SIZE
    for slot, kv_head in enumerate(kv_heads):
        kv_at = pl.ds(kv_head * HEAD_SIZE, HEAD_SIZE)
        key_now = k_ref[:, kv_at]
        value_now = v_ref[:, kv_at]
        key_grad = jnp.zeros((span, HEAD_SIZE), jnp.float32)
        value_grad = jnp.zeros((span, HEAD_SIZE), jnp.float32)
        for member in range(group_width):
            q_at = pl.ds((slot * group_width + member) * HEAD_SIZE, HEAD_SIZE)
            query_now = q_ref[:, q_at]
            grad_now = g_ref[:, q_at]
            scores = jnp.einsum("sd,td->st", key_now, query_now, preferred_element_type=jnp.float32) * scale
            scores = jnp.where(visible, scores, -jnp.inf)
            top = jnp.max(scores, axis=0, keepdims=True)
            expo = jnp.exp(scores - top)
            probs = expo / jnp.sum(expo, axis=0, keepdims=True)
            dprobs = jnp.einsum("sd,td->st", value_now, grad_now, preferred_element_type=jnp.float32)
            delta = jnp.sum(probs * dprobs, axis=0, keepdims=True)
            dscores_low = (probs * (dprobs - delta)).astype(jnp.bfloat16)
            probs_low = probs.astype(jnp.bfloat16)
            value_grad = value_grad + jnp.einsum("st,td->sd", probs_low, grad_now, preferred_element_type=jnp.float32)
            key_grad = key_grad + jnp.einsum("st,td->sd", dscores_low, query_now, preferred_element_type=jnp.float32)
            query_grad = jnp.einsum("st,sd->td", dscores_low, key_now, preferred_element_type=jnp.float32) * scale
            dq_ref[:, q_at] = query_grad.astype(dq_ref.dtype)
        dkv_ref[:, pl.ds(slot * HEAD_SIZE, HEAD_SIZE)] = key_grad * scale
        dkv_ref[:, pl.ds(kv_cols + slot * HEAD_SIZE, HEAD_SIZE)] = value_grad


def window_grads(kv_heads, queries, key_window, value_window, out_grad, query_segments, key_segments):
    rows = queries.shape[0]
    span = key_window.shape[0]
    group_width = QUERY_HEADS // KEY_VALUE_HEADS
    q_cols = len(kv_heads) * group_width * HEAD_SIZE
    kv_cols = len(kv_heads) * HEAD_SIZE
    return pl.pallas_call(
        functools.partial(attention_kernel, kv_heads),
        grid=(1,),
        out_shape=(
            jax.ShapeDtypeStruct((rows, q_cols), jnp.bfloat16),
            jax.ShapeDtypeStruct((span, 2 * kv_cols), jnp.float32),
        ),
        in_specs=[
            pl.BlockSpec((rows, q_cols), lambda i: (0, kv_heads[0] // len(kv_heads))),
            pl.BlockSpec((rows, q_cols), lambda i: (0, kv_heads[0] // len(kv_heads))),
        ] + [pl.BlockSpec(memory_space=pltpu.VMEM)] * 4,
        out_specs=(pl.BlockSpec(memory_space=pltpu.VMEM), pl.BlockSpec(memory_space=pltpu.VMEM)),
        cost_estimate=pl.CostEstimate(
            flops=10 * rows * span * q_cols,
            transcendentals=rows * span * len(kv_heads) * group_width,
            bytes_accessed=4 * rows * q_cols * 2 + span * 8 * kv_cols,
        ),
    )(queries, out_grad, key_window, value_window, query_segments.reshape(1, rows), key_segments.reshape(span, 1))


def on_device(hidden_in, queries, keys, values, out_grad, segment_ids):
    rows_per_block = queries.shape[0]
    cycle_place = lax.axis_index(("ctx", "dp"))
    kv_width = keys.shape[1]
    prev_kv = shifted(jnp.concatenate([keys, values], 1), ("ctx", "dp"), 1)
    prev_hidden = shifted(hidden_in, ("ctx", "dp"), 1)
    key_span_window = jnp.concatenate([prev_kv[:, :kv_width], keys], 0)
    value_span_window = jnp.concatenate([prev_kv[:, kv_width:], values], 0)
    own_segments = lax.dynamic_slice_in_dim(
        segment_ids, cycle_place * rows_per_block, rows_per_block, 0
    )
    prev_segments = lax.dynamic_slice_in_dim(
        segment_ids, jnp.maximum(cycle_place - 1, 0) * rows_per_block, rows_per_block, 0
    )
    prev_segments = jnp.where(cycle_place > 0, prev_segments, -1)
    key_segments = jnp.concatenate([prev_segments, own_segments], 0)
    hidden_cols, lead = ordered_hidden(jnp.concatenate([prev_hidden, hidden_in], 0))
    labels, first, second = schedules()
    query_parts, weight_parts = [], []
    for kv_head in range(KEY_VALUE_HEADS):
        query_part, kv_part = window_grads(
            (kv_head,), queries, key_span_window, value_span_window, out_grad, own_segments, key_segments
        )
        query_parts.append(query_part)
        schedule = first if kv_head % 2 == 0 else second
        weight_parts.append(head_weight_grad(hidden_cols, kv_part, schedule, labels, lead))
    rows = weight_parts[0].shape[0] * weight_parts[0].shape[1]
    weight_parts = [w.reshape(rows, 2 * HEAD_SIZE) for w in weight_parts]
    weight_grad = jnp.concatenate(
        [w[:, :HEAD_SIZE] for w in weight_parts] + [w[:, HEAD_SIZE:] for w in weight_parts], 1
    )
    return (jnp.concatenate(query_parts, 1), weight_grad)


def solution(mesh):
    return jax.shard_map(
        on_device,
        mesh=mesh,
        in_specs=(
            P(("groups", "ctx", "dp"), None),
            P(("groups", "ctx", "dp"), None),
            P(("groups", "ctx", "dp"), None),
            P(("groups", "ctx", "dp"), None),
            P(("groups", "ctx", "dp"), None),
            P("groups"),
        ),
        out_specs=(P(("groups", "ctx", "dp"), None), P(("groups", "dp"), None)),
        check_vma=False,
    )
```
